128 devices in a mesh: ep: 64 (over x, z, y), dp: 2 (over core).
Axes of the slice: x: 4, y: 4, z: 4, core: 2. Of those that a mesh axis runs over, the one named last changes fastest.
Arguments:
- context: bfloat16 [8192, 4096], P('ep', 'dp'), may hold values from -6 to 6
- residual: bfloat16 [8192, 2048], P('ep'), may hold values from -6 to 6
- kv_new: bfloat16 [8192, 1024], P('ep', 'dp'), may hold values from -6 to 6
- moved_to: int32 [8192], P('ep'), may hold values from 0 to 8191, as said below
- choices: int32 [8192, 8], P('ep'), may hold values from 0 to 127, all different within a row; in each aligned block of 128 rows (0 to 127, 128 to 255, ...) at most 16 rows name the same one
- o_weight: bfloat16 [4096, 2048], P('dp'), may hold values from -0.09375 to 0.09375
- gain_mid: float32 [2048], replicated, may hold values from 0.1 to 1.9
- router_weight: bfloat16 [2048, 128], replicated, may hold values from -0.125 to 0.125
- w_gate: bfloat16 [128, 2048, 768], P(('ep', 'dp')), may hold values from -0.125 to 0.125
- w_up: bfloat16 [128, 2048, 768], P(('ep', 'dp')), may hold values from -0.125 to 0.125
- w_down: bfloat16 [128, 768, 2048], P(('ep', 'dp')), may hold values from -0.21875 to 0.21875
- gain_out: float32 [2048], replicated, may hold values from 0.1 to 1.9
Outputs:
- hidden_out: bfloat16 [8192, 2048], P('ep', 'dp')
- kv_moved: bfloat16 [8192, 1024], P('ep', 'dp')
The draws below stay inside these ranges and needn't reach their ends.
Inputs may be any that keep to these rules, and one draw needn't show every extreme that they name: moved_to is a permutation; the rows in positions s * 128 to (s + 1) * 128 - 1 move to exactly 2 positions in each block t * 128 + s * 2 to t * 128 + (s + 1) * 2 - 1, filling it. `choices`: in each aligned block of 128 rows of the new order no expert is named more than 16 times, a bound that some block reaches; the rows of one block of the initial order have no such bound.
All inputs are finite; a program needn't handle non-finite values.
Results may differ from the reference program's by a relative error of at most 0.0085.
Values may be sent and summed in bfloat16 or wider, within the bound.
No kernel may reach another device: no remote copies, remote signals or barrier semaphores. Data moves between devices by JAX's collectives and lax.ppermute only.
A program may use at most 128 MiB of HBM per device.

```python
import math
import jax
import jax.numpy as jnp
import numpy as np
from jax import lax

D = 2048
FF = 768
HEADS = 32
HEAD = 128
KV_HEADS = 4
TOP = 8
TOK_DEV = 128
TOKENS = 8192
EXPERTS = 128
CAP = 16
MIG = 2
N_EP = 64


def draw_moved_to(key, part):
    source_count = TOKENS // TOK_DEV
    sources = jnp.arange(source_count, dtype=jnp.int32)
    source_keys = jax.vmap(lambda source: jax.random.fold_in(jax.random.fold_in(key, 7), source))(sources)
    shuffles = jax.vmap(lambda source_key: jax.random.permutation(source_key, TOK_DEV))(source_keys).astype(jnp.int32)
    destination = shuffles // MIG
    slot_index = shuffles % MIG
    position = destination * TOK_DEV + sources[:, None] * MIG + slot_index
    return position.reshape(-1).astype(jnp.int32)


def steps_of(rng, extent, shards, smallest, high):
    gain, own = 1.0, jax.random.fold_in(rng, 6)
    for dim, shards_of in shards:
        steps = jnp.exp(jax.random.uniform(jax.random.fold_in(own, dim), (shards_of,), jnp.float32, smallest / len(shards), high / len(shards)))
        gain = gain * jnp.repeat(steps, extent[dim] // shards_of).reshape([-1 if axis == dim else 1 for axis in range(len(extent))])
    return gain


def shared_out(key, own, number, rows, number_of, top, most, slope):
    order = jax.random.permutation(key, number_of)
    heavy_load, usual = shares(number_of, rows * top, most, slope, True), shares(number_of, rows * top, most, slope, False)
    places = jnp.arange(number_of)

    def named(sizes, offset_by):
        used = int((sizes > 0).sum())
        fixed = max(1, used // 4)
        moved = fixed + (places - fixed + offset_by * (used - fixed)) % max(1, number_of - fixed)
        return jnp.zeros((number_of,), jnp.int32).at[order[jnp.where(places < fixed, places, moved)]].set(jnp.asarray(sizes, jnp.int32))

    sizes = jnp.where(number % 4 == 0, named(heavy_load, number // 4), named(usual, number - number // 4 - 1))
    mixed = jax.random.permutation(jax.random.fold_in(own, 3), number_of)
    donor, sink = mixed[0:number_of // 2 * 2:2], mixed[1:number_of // 2 * 2:2]
    slack = jnp.minimum(sizes[donor] - 1, most - sizes[sink]) // 2
    slack = jnp.where((donor == order[0]) | (sink == order[0]) | (sizes[sink] == 0), 0, jnp.maximum(slack, 0))
    moved = jax.random.randint(jax.random.fold_in(own, 4), (number_of // 2,), 0, 1 << 20) % (slack + 1)
    sizes = sizes.at[donor].add(-moved).at[sink].add(moved)
    members = jnp.searchsorted(jnp.cumsum(sizes), jnp.arange(rows * top), side="right").astype(jnp.int32)
    table = members.reshape(top, rows).T
    table = table[jax.random.permutation(jax.random.fold_in(own, 1), rows)]
    offset_by = jax.random.randint(jax.random.fold_in(own, 2), (rows, 1), 0, top)
    return jnp.take_along_axis(table, (jnp.arange(top)[None, :] + offset_by) % top, axis=1)


def shares(number_of, total, bound, skew, full):
    weights = [(1 << 20) // math.isqrt(standing ** skew) + 1 for standing in range(1, number_of + 1)]
    largest = bound if full else min(bound, max(-(-total // number_of), total * weights[0] // sum(weights)))
    least = 1 if total - largest >= number_of - 1 else 0
    counts, surplus = [largest] + [least] * (number_of - 1), total - largest - least * (number_of - 1)
    while surplus > 0:
        candidates = [i for i in range(1, number_of) if counts[i] < largest] or [i for i in range(1, number_of) if counts[i] < bound]
        whole, budget = sum([weights[i] for i in candidates]), surplus
        for i in candidates:
            more = min(bound - counts[i], max(1, budget * weights[i] // whole), surplus)
            counts[i] = counts[i] + more
            surplus = surplus - more
    return np.array(counts)


def normal_values(stream_key, shape, scale, bound, cuts=(), held_as=jnp.bfloat16):
    result = scale * jax.random.normal(stream_key, shape, jnp.float32)
    if cuts:
        result = result * steps_of(stream_key, shape, cuts, -0.22, 0.18)
    return jnp.clip(result, -bound, bound).astype(held_as)


def setup_inputs(seed: int = 0) -> dict:
    seeds = jax.random.split(jax.random.key(seed), 13)
    context = normal_values(seeds[0], (TOKENS, HEADS * HEAD), 1.0, 6.0, ((0, 64), (1, 2)))
    residual = normal_values(seeds[1], (TOKENS, D), 1.0, 6.0, ((0, 64),))
    kv_new = normal_values(seeds[2], (TOKENS, KV_HEADS * 2 * HEAD), 1.0, 6.0, ((0, 64), (1, 2)))
    moved_to = draw_moved_to(jax.random.fold_in(seeds[12], 71), 0)
    choices_keys = jax.random.split(jax.random.fold_in(seeds[4], 1), TOKENS // TOK_DEV)
    choices_turns = jax.random.permutation(jax.random.fold_in(seeds[4], 3), TOKENS // TOK_DEV)
    choices = jax.vmap(lambda own, number: shared_out(jax.random.fold_in(seeds[4], 2), own, number, TOK_DEV, EXPERTS, TOP, CAP, 2))(choices_keys, choices_turns).reshape((TOKENS, TOP))
    o_weight = normal_values(seeds[5], (HEADS * HEAD, D), (HEADS * HEAD) ** -0.5, 0.09375, ((0, 2),))
    gain_mid = jnp.clip(1.0 + 0.18 * jax.random.normal(seeds[6], (D,), jnp.float32), 0.1, 1.9)
    router_weight = normal_values(seeds[7], (D, EXPERTS), D ** -0.5, 0.125)
    w_gate = normal_values(seeds[8], (EXPERTS, D, FF), D ** -0.5, 0.125, ((0, 128),))
    w_up = normal_values(seeds[9], (EXPERTS, D, FF), D ** -0.5, 0.125, ((0, 128),))
    w_down = normal_values(seeds[10], (EXPERTS, FF, D), FF ** -0.5, 0.21875, ((0, 128),))
    gain_out = jnp.clip(1.0 + 0.18 * jax.random.normal(seeds[11], (D,), jnp.float32), 0.1, 1.9)
    return {"context": context, "residual": residual, "kv_new": kv_new, "moved_to": moved_to, "choices": choices, "o_weight": o_weight, "gain_mid": gain_mid, "router_weight": router_weight, "w_gate": w_gate, "w_up": w_up, "w_down": w_down, "gain_out": gain_out}


epsilon = 1e-06

def rms_norm(values_in, gain_vec):
    return values_in * lax.rsqrt(lax.optimization_barrier(jnp.mean(values_in * values_in, axis=-1, keepdims=True)) + epsilon) * gain_vec

def reference(context, residual, kv_new, moved_to, choices, o_weight, gain_mid, router_weight, w_gate, w_up, w_down, gain_out):
    stream = (residual.astype(jnp.float32) + jnp.dot(context, o_weight, preferred_element_type=jnp.float32)).astype(jnp.bfloat16)
    row_ids = jnp.arange(TOKENS, dtype=jnp.int32)
    anchor = jnp.zeros((TOKENS,), jnp.int32).at[moved_to].set(row_ids)
    stream = stream[anchor]
    kv_moved = kv_new[anchor]
    normed = rms_norm(stream.astype(jnp.float32), gain_mid).astype(jnp.bfloat16)
    logits = jnp.dot(normed, router_weight, preferred_element_type=jnp.float32)
    picked = jnp.take_along_axis(logits, choices, axis=1)
    scores = jnp.exp(picked)
    mixing = scores / lax.optimization_barrier(jnp.sum(scores, axis=1, keepdims=True))
    slot_limit = N_EP * CAP
    padded = jnp.concatenate([normed, jnp.zeros((1, D), jnp.bfloat16)], axis=0)

    def expert_step(totals, inputs):
        expert_index, gate_w, up_w, down_w = inputs
        matches = choices == expert_index
        chosen = jnp.any(matches, axis=1)
        weight = lax.optimization_barrier(jnp.sum(jnp.where(matches, mixing, jnp.zeros_like(mixing)), axis=1))
        slot_rank = jnp.cumsum(chosen.astype(jnp.int32)) - 1
        where_to = jnp.where(chosen, slot_rank, slot_limit).astype(jnp.int32)
        slot_rows = jnp.full((slot_limit + 1,), TOKENS, jnp.int32).at[where_to].set(row_ids)[:slot_limit]
        gathered = padded[slot_rows]
        gate_out = jnp.dot(gathered, gate_w, preferred_element_type=jnp.float32)
        up_out = jnp.dot(gathered, up_w, preferred_element_type=jnp.float32)
        active = (jax.nn.silu(gate_out) * up_out).astype(jnp.bfloat16)
        expert_out = jnp.dot(active, down_w, preferred_element_type=jnp.float32).astype(jnp.bfloat16)
        weight_pad = jnp.concatenate([weight, jnp.zeros((1,), weight.dtype)])
        slot_weight = weight_pad[slot_rows]
        totals = totals.at[slot_rows].add(expert_out.astype(jnp.float32) * slot_weight[:, None])
        return (totals, None)
    start_total = jnp.zeros((TOKENS + 1, D), jnp.float32)
    totals, unused = lax.scan(expert_step, start_total, (jnp.arange(EXPERTS, dtype=jnp.int32), w_gate, w_up, w_down))
    combined = stream.astype(jnp.float32) + totals[:TOKENS]
    result_rows = rms_norm(combined, gain_out).astype(jnp.bfloat16)
    return (result_rows[moved_to], kv_moved)
```

```python
import jax
import jax.numpy as jnp
from jax import lax
from jax.sharding import PartitionSpec as P

epsilon = 1e-06


def local(
    context,
    residual,
    kv_new,
    moved_to,
    choices,
    o_weight,
    gain_mid,
    router_weight,
    w_gate,
    w_up,
    w_down,
    gain_out,
):
    peer_count = lax.axis_size("ep")
    dp_count = lax.axis_size("dp")
    my_side = lax.axis_index("dp")
    row_count = moved_to.shape[0]
    share_rows = row_count // peer_count
    model_width = gain_out.shape[0]
    col_width = model_width // dp_count
    expert_count = router_weight.shape[1]
    top_count = choices.shape[1]
    capacity = 2 * row_count * top_count // expert_count
    slot_limit = peer_count * capacity
    my_index = lax.axis_index("ep")

    partial = jnp.dot(context, o_weight, preferred_element_type=jnp.float32)
    summed = lax.psum_scatter(partial, "dp", scatter_dimension=1, tiled=True)
    res_cols = lax.dynamic_slice_in_dim(residual, my_side * col_width, col_width, 1)
    stream_half = (res_cols.astype(jnp.float32) + summed).astype(jnp.bfloat16)

    target = moved_to // row_count
    placed = target * share_rows + moved_to % row_count - my_index * share_rows
    lanes = jnp.arange(row_count, dtype=jnp.int32)
    perm = (placed[None, :] == lanes[:, None]).astype(jnp.bfloat16)
    payload = jnp.concatenate([stream_half, kv_new], axis=1)
    packed = jnp.dot(perm, payload, preferred_element_type=jnp.float32).astype(jnp.bfloat16)
    moved = lax.all_to_all(
        packed.reshape(peer_count, share_rows, -1), "ep", 0, 0, tiled=True
    ).reshape(row_count, -1)
    stream_mine = moved[:, :col_width]
    kv_moved = moved[:, col_width:]
    stream = lax.all_gather(stream_mine, "dp", axis=1, tiled=True)

    stream_f = stream.astype(jnp.float32)
    normed = (
        stream_f
        * lax.rsqrt(jnp.mean(stream_f * stream_f, axis=-1, keepdims=True) + epsilon)
        * gain_mid
    ).astype(jnp.bfloat16)
    logits = jnp.dot(normed, router_weight, preferred_element_type=jnp.float32)
    picked = jnp.take_along_axis(logits, choices, axis=1)
    scores = jnp.exp(picked)
    mixing = scores / jnp.sum(scores, axis=1, keepdims=True)

    owned = choices % dp_count == my_side
    expert_iota = jnp.arange(expert_count, dtype=jnp.int32)
    onehot_hits = (choices[:, :, None] == expert_iota[None, None, :]).astype(jnp.int32)
    per_row = jnp.sum(onehot_hits, axis=1)
    before_rows = jnp.cumsum(per_row, axis=0) - per_row
    slot_rank = jnp.sum(onehot_hits * before_rows[:, None, :], axis=2)
    slot_index = jnp.where(owned, choices // dp_count * capacity + slot_rank, slot_limit)
    slot_iota = jnp.arange(slot_limit, dtype=jnp.int32)
    hit = slot_index[:, :, None] == slot_iota[None, None, :]
    route = jnp.any(hit, axis=1).astype(jnp.bfloat16)
    outgoing = lax.dot_general(
        route, normed, (((0,), (0,)), ((), ())), preferred_element_type=jnp.float32
    ).astype(jnp.bfloat16)

    arrived = lax.all_to_all(
        outgoing.reshape(peer_count, capacity, model_width), "ep", 0, 0, tiled=True
    )
    flat_rows = arrived.reshape(-1, model_width)
    gate_out = jnp.dot(flat_rows, w_gate[0], preferred_element_type=jnp.float32)
    up_out = jnp.dot(flat_rows, w_up[0], preferred_element_type=jnp.float32)
    active = (jax.nn.silu(gate_out) * up_out).astype(jnp.bfloat16)
    expert_out = jnp.dot(active, w_down[0], preferred_element_type=jnp.float32).astype(jnp.bfloat16)
    returned = lax.all_to_all(
        expert_out.reshape(arrived.shape), "ep", 0, 0, tiled=True
    ).reshape(slot_limit, model_width)

    share_mix = jnp.where(owned, mixing, jnp.zeros_like(mixing))
    weights = jnp.sum(jnp.where(hit, share_mix[:, :, None], 0.0), axis=1)
    w_hi = weights.astype(jnp.bfloat16)
    w_lo = (weights - w_hi.astype(jnp.float32)).astype(jnp.bfloat16)
    moe_part = jnp.dot(w_hi, returned, preferred_element_type=jnp.float32) + jnp.dot(
        w_lo, returned, preferred_element_type=jnp.float32
    )
    moe_cols = lax.psum_scatter(moe_part, "dp", scatter_dimension=1, tiled=True)
    combined = stream_mine.astype(jnp.float32) + moe_cols
    square_sum = lax.psum(jnp.sum(combined * combined, axis=-1, keepdims=True), "dp")
    gain_cols = lax.dynamic_slice_in_dim(gain_out, my_side * col_width, col_width, 0)
    result_cols = (
        combined * lax.rsqrt(square_sum / model_width + epsilon) * gain_cols
    ).astype(jnp.bfloat16)
    back = lax.all_to_all(
        result_cols.reshape(peer_count, share_rows, col_width), "ep", 0, 0, tiled=True
    ).reshape(row_count, col_width)
    hidden_out = lax.dot_general(
        perm, back, (((0,), (0,)), ((), ())), preferred_element_type=jnp.float32
    ).astype(jnp.bfloat16)
    return (hidden_out, kv_moved)


def solution(mesh):
    placed = (
        P("ep", "dp"),
        P("ep", None),
        P("ep", "dp"),
        P("ep"),
        P("ep", None),
        P("dp", None),
        P(),
        P(),
        P(("ep", "dp"), None, None),
        P(("ep", "dp"), None, None),
        P(("ep", "dp"), None, None),
        P(),
    )
    return jax.shard_map(
        local, mesh=mesh, in_specs=placed, out_specs=(P("ep", "dp"), P("ep", "dp")), check_vma=False
    )
```

```python
import jax
import jax.numpy as jnp
from jax import lax
from jax.sharding import PartitionSpec as P

epsilon = 1e-06


def local(
    context,
    residual,
    kv_new,
    moved_to,
    choices,
    o_weight,
    gain_mid,
    router_weight,
    w_gate,
    w_up,
    w_down,
    gain_out,
):
    peer_count = lax.axis_size("ep")
    dp_count = lax.axis_size("dp")
    my_side = lax.axis_index("dp")
    row_count = moved_to.shape[0]
    share_rows = row_count // peer_count
    model_width = gain_out.shape[0]
    col_width = model_width // dp_count
    expert_count = router_weight.shape[1]
    top_count = choices.shape[1]
    capacity = 2 * row_count * top_count // expert_count
    slot_limit = peer_count * capacity
    my_index = lax.axis_index("ep")

    def swap(x):
        return lax.ppermute(x, "dp", [(0, 1), (1, 0)])

    def own_cols(x):
        return lax.dynamic_slice_in_dim(x, my_side * col_width, col_width, 1)

    def other_cols(x):
        return lax.dynamic_slice_in_dim(x, (1 - my_side) * col_width, col_width, 1)

    partial = jnp.dot(context, o_weight, preferred_element_type=jnp.float32)
    summed = own_cols(partial) + swap(other_cols(partial))
    res_cols = lax.dynamic_slice_in_dim(residual, my_side * col_width, col_width, 1)
    stream_half = (res_cols.astype(jnp.float32) + summed).astype(jnp.bfloat16)

    target = moved_to // row_count
    placed = target * share_rows + moved_to % row_count - my_index * share_rows
    lanes = jnp.arange(row_count, dtype=jnp.int32)
    perm = (placed[None, :] == lanes[:, None]).astype(jnp.bfloat16)
    payload = jnp.concatenate([stream_half, kv_new], axis=1)
    packed = jnp.dot(perm, payload, preferred_element_type=jnp.float32).astype(jnp.bfloat16)
    moved = lax.all_to_all(
        packed.reshape(peer_count, share_rows, -1), "ep", 0, 0, tiled=True
    ).reshape(row_count, -1)
    stream_mine = moved[:, :col_width]
    kv_moved = moved[:, col_width:]
    stream_other = swap(stream_mine)
    stream = jnp.where(
        my_side == 0,
        jnp.concatenate([stream_mine, stream_other], axis=1),
        jnp.concatenate([stream_other, stream_mine], axis=1),
    )

    stream_f = stream.astype(jnp.float32)
    normed = (
        stream_f
        * lax.rsqrt(jnp.mean(stream_f * stream_f, axis=-1, keepdims=True) + epsilon)
        * gain_mid
    ).astype(jnp.bfloat16)
    logits = jnp.dot(normed, router_weight, preferred_element_type=jnp.float32)
    expert_iota = jnp.arange(expert_count, dtype=jnp.int32)
    onehot_bool = choices[:, :, None] == expert_iota[None, None, :]
    picked = jnp.sum(jnp.where(onehot_bool, logits[:, None, :], 0.0), axis=2)
    scores = jnp.exp(picked)
    mixing = scores / jnp.sum(scores, axis=1, keepdims=True)

    owned = choices % dp_count == my_side
    onehot_hits = onehot_bool.astype(jnp.int32)
    per_row = jnp.sum(onehot_hits, axis=1)
    before_rows = jnp.cumsum(per_row, axis=0) - per_row
    slot_rank = jnp.sum(onehot_hits * before_rows[:, None, :], axis=2)
    slot_index = jnp.where(owned, choices // dp_count * capacity + slot_rank, slot_limit)
    slot_iota = jnp.arange(slot_limit, dtype=jnp.int32)
    hit = slot_index[:, :, None] == slot_iota[None, None, :]
    route = jnp.any(hit, axis=1).astype(jnp.bfloat16)
    outgoing = lax.dot_general(
        route, normed, (((0,), (0,)), ((), ())), preferred_element_type=jnp.float32
    ).astype(jnp.bfloat16)

    arrived = lax.all_to_all(
        outgoing.reshape(peer_count, capacity, model_width), "ep", 0, 0, tiled=True
    )
    flat_rows = arrived.reshape(-1, model_width)
    gate_out = jnp.dot(flat_rows, w_gate[0], preferred_element_type=jnp.float32)
    up_out = jnp.dot(flat_rows, w_up[0], preferred_element_type=jnp.float32)
    active = (jax.nn.silu(gate_out) * up_out).astype(jnp.bfloat16)
    expert_out = jnp.dot(active, w_down[0], preferred_element_type=jnp.float32).astype(jnp.bfloat16)
    returned = lax.all_to_all(
        expert_out.reshape(arrived.shape), "ep", 0, 0, tiled=True
    ).reshape(slot_limit, model_width)

    share_mix = jnp.where(owned, mixing, jnp.zeros_like(mixing))
    weights = jnp.sum(jnp.where(hit, share_mix[:, :, None], 0.0), axis=1)
    w_hi = weights.astype(jnp.bfloat16)
    w_lo = (weights - w_hi.astype(jnp.float32)).astype(jnp.bfloat16)
    both = jnp.dot(
        jnp.concatenate([w_hi, w_lo], axis=0), returned, preferred_element_type=jnp.float32
    )
    moe_part = both[:row_count] + both[row_count:]
    moe_cols = own_cols(moe_part) + swap(other_cols(moe_part))
    combined = stream_mine.astype(jnp.float32) + moe_cols
    own_square = jnp.sum(combined * combined, axis=-1, keepdims=True)
    square_sum = own_square + swap(own_square)
    gain_cols = lax.dynamic_slice_in_dim(gain_out, my_side * col_width, col_width, 0)
    result_cols = (
        combined * lax.rsqrt(square_sum / model_width + epsilon) * gain_cols
    ).astype(jnp.bfloat16)
    back = lax.all_to_all(
        result_cols.reshape(peer_count, share_rows, col_width), "ep", 0, 0, tiled=True
    ).reshape(row_count, col_width)
    hidden_out = lax.dot_general(
        perm, back, (((0,), (0,)), ((), ())), preferred_element_type=jnp.float32
    ).astype(jnp.bfloat16)
    return (hidden_out, kv_moved)


def solution(mesh):
    placed = (
        P("ep", "dp"),
        P("ep", None),
        P("ep", "dp"),
        P("ep"),
        P("ep", None),
        P("dp", None),
        P(),
        P(),
        P(("ep", "dp"), None, None),
        P(("ep", "dp"), None, None),
        P(("ep", "dp"), None, None),
        P(),
    )
    return jax.shard_map(
        local, mesh=mesh, in_specs=placed, out_specs=(P("ep", "dp"), P("ep", "dp")), check_vma=False
    )
```

```python
import jax
import jax.numpy as jnp
from jax import lax
from jax.sharding import PartitionSpec as P

epsilon = 1e-06


def local(
    context,
    residual,
    kv_new,
    moved_to,
    choices,
    o_weight,
    gain_mid,
    router_weight,
    w_gate,
    w_up,
    w_down,
    gain_out,
):
    peer_count = lax.axis_size("ep")
    dp_count = lax.axis_size("dp")
    my_side = lax.axis_index("dp")
    row_count = moved_to.shape[0]
    share_rows = row_count // peer_count
    model_width = gain_out.shape[0]
    col_width = model_width // dp_count
    expert_count = router_weight.shape[1]
    top_count = choices.shape[1]
    capacity = 2 * row_count * top_count // expert_count
    slot_limit = peer_count * capacity
    my_index = lax.axis_index("ep")

    def swap(x):
        return lax.ppermute(x, "dp", [(0, 1), (1, 0)])

    def own_cols(x):
        return lax.dynamic_slice_in_dim(x, my_side * col_width, col_width, 1)

    def other_cols(x):
        return lax.dynamic_slice_in_dim(x, (1 - my_side) * col_width, col_width, 1)

    w_other = lax.dynamic_slice_in_dim(o_weight, (1 - my_side) * col_width, col_width, 1)
    w_own = lax.dynamic_slice_in_dim(o_weight, my_side * col_width, col_width, 1)
    partial_other = jnp.dot(context, w_other, preferred_element_type=jnp.float32)
    sent_other = swap(partial_other)
    partial_own = jnp.dot(context, w_own, preferred_element_type=jnp.float32)
    summed = partial_own + sent_other
    res_cols = lax.dynamic_slice_in_dim(residual, my_side * col_width, col_width, 1)
    stream_half = (res_cols.astype(jnp.float32) + summed).astype(jnp.bfloat16)

    target = moved_to // row_count
    placed = target * share_rows + moved_to % row_count - my_index * share_rows
    lanes = jnp.arange(row_count, dtype=jnp.int32)
    perm = (placed[None, :] == lanes[:, None]).astype(jnp.bfloat16)
    payload = jnp.concatenate([stream_half, kv_new], axis=1)
    packed = jnp.dot(perm, payload, preferred_element_type=jnp.float32).astype(jnp.bfloat16)
    moved = lax.all_to_all(
        packed.reshape(peer_count, share_rows, -1), "ep", 0, 0, tiled=True
    ).reshape(row_count, -1)
    stream_mine = moved[:, :col_width]
    kv_moved = moved[:, col_width:]
    stream_other = swap(stream_mine)
    stream = jnp.where(
        my_side == 0,
        jnp.concatenate([stream_mine, stream_other], axis=1),
        jnp.concatenate([stream_other, stream_mine], axis=1),
    )

    stream_f = stream.astype(jnp.float32)
    normed = (
        stream_f
        * lax.rsqrt(jnp.mean(stream_f * stream_f, axis=-1, keepdims=True) + epsilon)
        * gain_mid
    ).astype(jnp.bfloat16)
    logits = jnp.dot(normed, router_weight, preferred_element_type=jnp.float32)
    expert_iota = jnp.arange(expert_count, dtype=jnp.int32)
    onehot_bool = choices[:, :, None] == expert_iota[None, None, :]
    picked = jnp.sum(jnp.where(onehot_bool, logits[:, None, :], 0.0), axis=2)
    scores = jnp.exp(picked)
    mixing = scores / jnp.sum(scores, axis=1, keepdims=True)

    side_experts = jnp.arange(peer_count, dtype=jnp.int32) * dp_count + my_side
    match = choices[:, :, None] == side_experts[None, None, :]
    mine = jnp.any(match, axis=1)
    mine_count = mine.astype(jnp.int32)
    before = jnp.cumsum(mine_count, axis=0) - mine_count
    rank_iota = jnp.arange(capacity, dtype=jnp.int32)
    route3 = mine[:, :, None] & (before[:, :, None] == rank_iota[None, None, :])
    route = route3.reshape(row_count, slot_limit).astype(jnp.bfloat16)
    outgoing = lax.dot_general(
        route, normed, (((0,), (0,)), ((), ())), preferred_element_type=jnp.float32
    ).astype(jnp.bfloat16)

    arrived = lax.all_to_all(
        outgoing.reshape(peer_count, capacity, model_width), "ep", 0, 0, tiled=True
    )
    flat_rows = arrived.reshape(-1, model_width)
    gate_out = jnp.dot(flat_rows, w_gate[0], preferred_element_type=jnp.float32)
    up_out = jnp.dot(flat_rows, w_up[0], preferred_element_type=jnp.float32)
    active = (jax.nn.silu(gate_out) * up_out).astype(jnp.bfloat16)
    expert_out = jnp.dot(active, w_down[0], preferred_element_type=jnp.float32).astype(jnp.bfloat16)
    returned = lax.all_to_all(
        expert_out.reshape(arrived.shape), "ep", 0, 0, tiled=True
    ).reshape(slot_limit, model_width)

    chosen_mix = jnp.sum(jnp.where(match, mixing[:, :, None], 0.0), axis=1)
    weights = jnp.where(route3, chosen_mix[:, :, None], 0.0).reshape(row_count, slot_limit)
    w_hi = weights.astype(jnp.bfloat16)
    w_lo = (weights - w_hi.astype(jnp.float32)).astype(jnp.bfloat16)
    stacked = jnp.concatenate([w_hi, w_lo], axis=0)

    def mix_cols(cols):
        both = jnp.dot(stacked, cols, preferred_element_type=jnp.float32)
        return both[:row_count] + both[row_count:]

    sent_moe = swap(mix_cols(other_cols(returned)))
    moe_cols = mix_cols(own_cols(returned)) + sent_moe
    combined = stream_mine.astype(jnp.float32) + moe_cols
    own_square = jnp.sum(combined * combined, axis=-1, keepdims=True)
    square_sum = own_square + swap(own_square)
    gain_cols = lax.dynamic_slice_in_dim(gain_out, my_side * col_width, col_width, 0)
    result_cols = (
        combined * lax.rsqrt(square_sum / model_width + epsilon) * gain_cols
    ).astype(jnp.bfloat16)
    back = lax.all_to_all(
        result_cols.reshape(peer_count, share_rows, col_width), "ep", 0, 0, tiled=True
    ).reshape(row_count, col_width)
    hidden_out = lax.dot_general(
        perm, back, (((0,), (0,)), ((), ())), preferred_element_type=jnp.float32
    ).astype(jnp.bfloat16)
    return (hidden_out, kv_moved)


def solution(mesh):
    placed = (
        P("ep", "dp"),
        P("ep", None),
        P("ep", "dp"),
        P("ep"),
        P("ep", None),
        P("dp", None),
        P(),
        P(),
        P(("ep", "dp"), None, None),
        P(("ep", "dp"), None, None),
        P(("ep", "dp"), None, None),
        P(),
    )
    return jax.shard_map(
        local, mesh=mesh, in_specs=placed, out_specs=(P("ep", "dp"), P("ep", "dp")), check_vma=False
    )
```

```python
import jax
import jax.numpy as jnp
from jax import lax
from jax.sharding import PartitionSpec as P

epsilon = 1e-06


def local(
    context,
    residual,
    kv_new,
    moved_to,
    choices,
    o_weight,
    gain_mid,
    router_weight,
    w_gate,
    w_up,
    w_down,
    gain_out,
):
    peer_count = lax.axis_size("ep")
    dp_count = lax.axis_size("dp")
    my_side = lax.axis_index("dp")
    row_count = moved_to.shape[0]
    share_rows = row_count // peer_count
    model_width = gain_out.shape[0]
    col_width = model_width // dp_count
    expert_count = router_weight.shape[1]
    top_count = choices.shape[1]
    capacity = 2 * row_count * top_count // expert_count
    slot_limit = peer_count * capacity
    my_index = lax.axis_index("ep")

    def swap(x):
        return lax.ppermute(x, "dp", [(0, 1), (1, 0)])

    def own_cols(x):
        return lax.dynamic_slice_in_dim(x, my_side * col_width, col_width, 1)

    def other_cols(x):
        return lax.dynamic_slice_in_dim(x, (1 - my_side) * col_width, col_width, 1)

    partial = jnp.dot(context, o_weight, preferred_element_type=jnp.float32)
    summed = own_cols(partial) + swap(other_cols(partial))
    res_cols = lax.dynamic_slice_in_dim(residual, my_side * col_width, col_width, 1)
    stream_half = (res_cols.astype(jnp.float32) + summed).astype(jnp.bfloat16)

    target = moved_to // row_count
    placed = target * share_rows + moved_to % row_count - my_index * share_rows
    lanes = jnp.arange(row_count, dtype=jnp.int32)
    perm = (placed[None, :] == lanes[:, None]).astype(jnp.bfloat16)
    payload = jnp.concatenate([stream_half, kv_new], axis=1)
    packed = jnp.dot(perm, payload, preferred_element_type=jnp.float32).astype(jnp.bfloat16)
    moved = lax.all_to_all(
        packed.reshape(peer_count, share_rows, -1), "ep", 0, 0, tiled=True
    ).reshape(row_count, -1)
    side_experts = jnp.arange(peer_count, dtype=jnp.int32) * dp_count + my_side
    match = choices[:, :, None] == side_experts[None, None, :]
    mine = jnp.any(match, axis=1)
    earlier = (lanes[None, :] < lanes[:, None]).astype(jnp.bfloat16)
    before = jnp.dot(earlier, mine.astype(jnp.bfloat16), preferred_element_type=jnp.float32)
    rank_iota = jnp.arange(capacity, dtype=jnp.float32)
    route3 = mine[:, :, None] & (before[:, :, None] == rank_iota[None, None, :])
    route = route3.reshape(row_count, slot_limit).astype(jnp.bfloat16)
    moved, route = lax.optimization_barrier((moved, route))
    stream_mine = moved[:, :col_width]
    kv_moved = moved[:, col_width:]
    stream_other = swap(stream_mine)
    stream = jnp.where(
        my_side == 0,
        jnp.concatenate([stream_mine, stream_other], axis=1),
        jnp.concatenate([stream_other, stream_mine], axis=1),
    )

    stream_f = stream.astype(jnp.float32)
    normed = (
        stream_f
        * lax.rsqrt(jnp.mean(stream_f * stream_f, axis=-1, keepdims=True) + epsilon)
        * gain_mid
    ).astype(jnp.bfloat16)
    logits = jnp.dot(normed, router_weight, preferred_element_type=jnp.float32)
    expert_iota = jnp.arange(expert_count, dtype=jnp.int32)
    onehot_bool = choices[:, :, None] == expert_iota[None, None, :]
    picked = jnp.sum(jnp.where(onehot_bool, logits[:, None, :], 0.0), axis=2)
    scores = jnp.exp(picked)
    mixing = scores / jnp.sum(scores, axis=1, keepdims=True)

    outgoing = lax.dot_general(
        route, normed, (((0,), (0,)), ((), ())), preferred_element_type=jnp.float32
    ).astype(jnp.bfloat16)

    arrived = lax.all_to_all(
        outgoing.reshape(peer_count, capacity, model_width), "ep", 0, 0, tiled=True
    )
    flat_rows = arrived.reshape(-1, model_width)
    gate_out = jnp.dot(flat_rows, w_gate[0], preferred_element_type=jnp.float32)
    up_out = jnp.dot(flat_rows, w_up[0], preferred_element_type=jnp.float32)
    active = (jax.nn.silu(gate_out) * up_out).astype(jnp.bfloat16)
    expert_out = jnp.dot(active, w_down[0], preferred_element_type=jnp.float32).astype(jnp.bfloat16)
    returned = lax.all_to_all(
        expert_out.reshape(arrived.shape), "ep", 0, 0, tiled=True
    ).reshape(slot_limit, model_width)

    chosen_mix = jnp.sum(jnp.where(match, mixing[:, :, None], 0.0), axis=1)
    weights = jnp.where(route3, chosen_mix[:, :, None], 0.0).reshape(row_count, slot_limit)
    w_hi = weights.astype(jnp.bfloat16)
    w_lo = (weights - w_hi.astype(jnp.float32)).astype(jnp.bfloat16)
    both = jnp.dot(
        jnp.concatenate([w_hi, w_lo], axis=0), returned, preferred_element_type=jnp.float32
    )
    moe_part = both[:row_count] + both[row_count:]
    moe_cols = own_cols(moe_part) + swap(other_cols(moe_part))
    combined = stream_mine.astype(jnp.float32) + moe_cols
    own_square = jnp.sum(combined * combined, axis=-1, keepdims=True)
    square_sum = own_square + swap(own_square)
    gain_cols = lax.dynamic_slice_in_dim(gain_out, my_side * col_width, col_width, 0)
    result_cols = (
        combined * lax.rsqrt(square_sum / model_width + epsilon) * gain_cols
    ).astype(jnp.bfloat16)
    back = lax.all_to_all(
        result_cols.reshape(peer_count, share_rows, col_width), "ep", 0, 0, tiled=True
    ).reshape(row_count, col_width)
    hidden_out = lax.dot_general(
        perm, back, (((0,), (0,)), ((), ())), preferred_element_type=jnp.float32
    ).astype(jnp.bfloat16)
    return (hidden_out, kv_moved)


def solution(mesh):
    placed = (
        P("ep", "dp"),
        P("ep", None),
        P("ep", "dp"),
        P("ep"),
        P("ep", None),
        P("dp", None),
        P(),
        P(),
        P(("ep", "dp"), None, None),
        P(("ep", "dp"), None, None),
        P(("ep", "dp"), None, None),
        P(),
    )
    return jax.shard_map(
        local, mesh=mesh, in_specs=placed, out_specs=(P("ep", "dp"), P("ep", "dp")), check_vma=False
    )
```

```python
import jax
import jax.numpy as jnp
from jax import lax
from jax.sharding import PartitionSpec as P

epsilon = 1e-06


def local(
    context,
    residual,
    kv_new,
    moved_to,
    choices,
    o_weight,
    gain_mid,
    router_weight,
    w_gate,
    w_up,
    w_down,
    gain_out,
):
    peer_count = lax.axis_size("ep")
    dp_count = lax.axis_size("dp")
    my_side = lax.axis_index("dp")
    row_count = moved_to.shape[0]
    share_rows = row_count // peer_count
    model_width = gain_out.shape[0]
    col_width = model_width // dp_count
    expert_count = router_weight.shape[1]
    top_count = choices.shape[1]
    capacity = 2 * row_count * top_count // expert_count
    slot_limit = peer_count * capacity
    my_index = lax.axis_index("ep")

    def swap(x):
        return lax.ppermute(x, "dp", [(0, 1), (1, 0)])

    def own_cols(x):
        return lax.dynamic_slice_in_dim(x, my_side * col_width, col_width, 1)

    def other_cols(x):
        return lax.dynamic_slice_in_dim(x, (1 - my_side) * col_width, col_width, 1)

    partial = jnp.dot(context, o_weight, preferred_element_type=jnp.float32)
    summed = own_cols(partial) + swap(other_cols(partial))
    res_cols = lax.dynamic_slice_in_dim(residual, my_side * col_width, col_width, 1)
    stream_half = (res_cols.astype(jnp.float32) + summed).astype(jnp.bfloat16)

    target = moved_to // row_count
    placed = target * share_rows + moved_to % row_count - my_index * share_rows
    lanes = jnp.arange(row_count, dtype=jnp.int32)
    slots = lanes.reshape(peer_count, share_rows)
    perm3 = (placed[None, None, :] == slots[:, :, None]).astype(jnp.bfloat16)
    payload = jnp.concatenate([stream_half, kv_new], axis=1)
    packed = lax.dot_general(
        perm3, payload, (((2,), (0,)), ((), ())), preferred_element_type=jnp.float32
    ).astype(jnp.bfloat16)
    moved = lax.all_to_all(packed, "ep", 0, 0, tiled=True).reshape(row_count, -1)
    side_experts = jnp.arange(peer_count, dtype=jnp.int32) * dp_count + my_side
    match = choices[:, :, None] == side_experts[None, None, :]
    mine = jnp.any(match, axis=1)
    earlier = (lanes[None, :] < lanes[:, None]).astype(jnp.bfloat16)
    before = jnp.dot(earlier, mine.astype(jnp.bfloat16), preferred_element_type=jnp.float32)
    rank_iota = jnp.arange(capacity, dtype=jnp.float32)
    route3 = mine[:, :, None] & (before[:, :, None] == rank_iota[None, None, :])
    route = route3.reshape(row_count, slot_limit).astype(jnp.bfloat16)
    moved, route = lax.optimization_barrier((moved, route))
    stream_mine = moved[:, :col_width]
    kv_moved = moved[:, col_width:]
    stream_other = swap(stream_mine)
    stream = jnp.where(
        my_side == 0,
        jnp.concatenate([stream_mine, stream_other], axis=1),
        jnp.concatenate([stream_other, stream_mine], axis=1),
    )

    stream_f = stream.astype(jnp.float32)
    normed = (
        stream_f
        * lax.rsqrt(jnp.mean(stream_f * stream_f, axis=-1, keepdims=True) + epsilon)
        * gain_mid
    ).astype(jnp.bfloat16)
    logits = jnp.dot(normed, router_weight, preferred_element_type=jnp.float32)
    expert_iota = jnp.arange(expert_count, dtype=jnp.int32)
    onehot_bool = choices[:, :, None] == expert_iota[None, None, :]
    picked = jnp.sum(jnp.where(onehot_bool, logits[:, None, :], 0.0), axis=2)
    scores = jnp.exp(picked)
    mixing = scores / jnp.sum(scores, axis=1, keepdims=True)

    outgoing = lax.dot_general(
        route, normed, (((0,), (0,)), ((), ())), preferred_element_type=jnp.float32
    ).astype(jnp.bfloat16)

    arrived = lax.all_to_all(
        outgoing.reshape(peer_count, capacity, model_width), "ep", 0, 0, tiled=True
    )
    flat_rows = arrived.reshape(-1, model_width)
    gate_out = jnp.dot(flat_rows, w_gate[0], preferred_element_type=jnp.float32)
    up_out = jnp.dot(flat_rows, w_up[0], preferred_element_type=jnp.float32)
    active = (jax.nn.silu(gate_out) * up_out).astype(jnp.bfloat16)
    expert_out = jnp.dot(active, w_down[0], preferred_element_type=jnp.float32).astype(jnp.bfloat16)
    returned = lax.all_to_all(
        expert_out.reshape(arrived.shape), "ep", 0, 0, tiled=True
    ).reshape(slot_limit, model_width)

    chosen_mix = jnp.sum(jnp.where(match, mixing[:, :, None], 0.0), axis=1)
    weights = jnp.where(route3, chosen_mix[:, :, None], 0.0).reshape(row_count, slot_limit)
    moe_part = jnp.dot(
        weights.astype(jnp.bfloat16), returned, preferred_element_type=jnp.float32
    )
    moe_cols = own_cols(moe_part) + swap(other_cols(moe_part))
    combined = stream_mine.astype(jnp.float32) + moe_cols
    own_square = jnp.sum(combined * combined, axis=-1, keepdims=True)
    square_sum = own_square + swap(own_square)
    gain_cols = lax.dynamic_slice_in_dim(gain_out, my_side * col_width, col_width, 0)
    result_cols = (
        combined * lax.rsqrt(square_sum / model_width + epsilon) * gain_cols
    ).astype(jnp.bfloat16)
    back = lax.all_to_all(
        result_cols.reshape(peer_count, share_rows, col_width), "ep", 0, 0, tiled=True
    )
    hidden_out = lax.dot_general(
        perm3, back, (((0, 1), (0, 1)), ((), ())), preferred_element_type=jnp.float32
    ).astype(jnp.bfloat16)
    return (hidden_out, kv_moved)


def solution(mesh):
    placed = (
        P("ep", "dp"),
        P("ep", None),
        P("ep", "dp"),
        P("ep"),
        P("ep", None),
        P("dp", None),
        P(),
        P(),
        P(("ep", "dp"), None, None),
        P(("ep", "dp"), None, None),
        P(("ep", "dp"), None, None),
        P(),
    )
    return jax.shard_map(
        local, mesh=mesh, in_specs=placed, out_specs=(P("ep", "dp"), P("ep", "dp")), check_vma=False
    )
```

```python
import jax
import jax.numpy as jnp
from jax import lax
from jax.sharding import PartitionSpec as P

epsilon = 1e-06


def local(
    context,
    residual,
    kv_new,
    moved_to,
    choices,
    o_weight,
    gain_mid,
    router_weight,
    w_gate,
    w_up,
    w_down,
    gain_out,
):
    peer_count = lax.axis_size("ep")
    dp_count = lax.axis_size("dp")
    my_side = lax.axis_index("dp")
    row_count = moved_to.shape[0]
    share_rows = row_count // peer_count
    model_width = gain_out.shape[0]
    col_width = model_width // dp_count
    expert_count = router_weight.shape[1]
    top_count = choices.shape[1]
    capacity = 2 * row_count * top_count // expert_count
    slot_limit = peer_count * capacity
    my_index = lax.axis_index("ep")

    def swap(x):
        return lax.ppermute(x, "dp", [(0, 1), (1, 0)])

    def own_cols(x):
        return lax.dynamic_slice_in_dim(x, my_side * col_width, col_width, 1)

    def other_cols(x):
        return lax.dynamic_slice_in_dim(x, (1 - my_side) * col_width, col_width, 1)

    partial = jnp.dot(context, o_weight, preferred_element_type=jnp.float32)
    summed = own_cols(partial) + swap(other_cols(partial))
    res_cols = lax.dynamic_slice_in_dim(residual, my_side * col_width, col_width, 1)
    stream_half = (res_cols.astype(jnp.float32) + summed).astype(jnp.bfloat16)

    target = moved_to // row_count
    placed = target * share_rows + moved_to % row_count - my_index * share_rows
    lanes = jnp.arange(row_count, dtype=jnp.int32)
    slots = lanes.reshape(peer_count, share_rows)
    perm3 = (placed[None, None, :] == slots[:, :, None]).astype(jnp.bfloat16)
    payload = jnp.concatenate([stream_half, kv_new], axis=1)
    packed = lax.dot_general(
        perm3, payload, (((2,), (0,)), ((), ())), preferred_element_type=jnp.float32
    ).astype(jnp.bfloat16)
    moved = lax.all_to_all(packed, "ep", 0, 0, tiled=True).reshape(row_count, -1)
    side_experts = jnp.arange(peer_count, dtype=jnp.int32) * dp_count + my_side
    match = choices[:, :, None] == side_experts[None, None, :]
    mine = jnp.any(match, axis=1)
    earlier = (lanes[None, :] < lanes[:, None]).astype(jnp.bfloat16)
    before = jnp.dot(earlier, mine.astype(jnp.bfloat16), preferred_element_type=jnp.float32)
    rank_iota = jnp.arange(capacity, dtype=jnp.float32)
    route3 = mine[:, :, None] & (before[:, :, None] == rank_iota[None, None, :])
    route = route3.reshape(row_count, slot_limit).astype(jnp.bfloat16)
    moved, route = lax.optimization_barrier((moved, route))
    stream_mine = moved[:, :col_width]
    kv_moved = moved[:, col_width:]
    stream_other = swap(stream_mine)
    stream = jnp.where(
        my_side == 0,
        jnp.concatenate([stream_mine, stream_other], axis=1),
        jnp.concatenate([stream_other, stream_mine], axis=1),
    )

    stream_f = stream.astype(jnp.float32)
    normed = (
        stream_f
        * lax.rsqrt(jnp.mean(stream_f * stream_f, axis=-1, keepdims=True) + epsilon)
        * gain_mid
    ).astype(jnp.bfloat16)
    logits = jnp.dot(normed, router_weight, preferred_element_type=jnp.float32)
    expert_iota = jnp.arange(expert_count, dtype=jnp.int32)
    onehot_bool = choices[:, :, None] == expert_iota[None, None, :]
    picked = jnp.sum(jnp.where(onehot_bool, logits[:, None, :], 0.0), axis=2)
    scores = jnp.exp(picked)
    mixing = scores / jnp.sum(scores, axis=1, keepdims=True)

    outgoing = lax.dot_general(
        route, normed, (((0,), (0,)), ((), ())), preferred_element_type=jnp.float32
    ).astype(jnp.bfloat16)

    arrived = lax.all_to_all(
        outgoing.reshape(peer_count, capacity, model_width), "ep", 0, 0, tiled=True
    )
    flat_rows = arrived.reshape(-1, model_width)
    gate_out = jnp.dot(flat_rows, w_gate[0], preferred_element_type=jnp.float32)
    up_out = jnp.dot(flat_rows, w_up[0], preferred_element_type=jnp.float32)
    active = (jax.nn.silu(gate_out) * up_out).astype(jnp.bfloat16)
    expert_out = jnp.dot(active, w_down[0], preferred_element_type=jnp.float32).astype(jnp.bfloat16)
    returned = lax.all_to_all(
        expert_out.reshape(arrived.shape), "ep", 0, 0, tiled=True
    ).reshape(slot_limit, model_width)

    chosen_mix = jnp.sum(jnp.where(match, mixing[:, :, None], 0.0), axis=1)
    weights = jnp.where(route3, chosen_mix[:, :, None], 0.0).reshape(row_count, slot_limit)
    moe_part = jnp.dot(
        weights.astype(jnp.bfloat16), returned, preferred_element_type=jnp.float32
    )
    moe_other = swap(moe_part.astype(jnp.bfloat16))
    combined_full = stream_f + moe_part + moe_other.astype(jnp.float32)
    square_sum = jnp.sum(combined_full * combined_full, axis=-1, keepdims=True)
    combined = own_cols(combined_full)
    gain_cols = lax.dynamic_slice_in_dim(gain_out, my_side * col_width, col_width, 0)
    result_cols = (
        combined * lax.rsqrt(square_sum / model_width + epsilon) * gain_cols
    ).astype(jnp.bfloat16)
    back = lax.all_to_all(
        result_cols.reshape(peer_count, share_rows, col_width), "ep", 0, 0, tiled=True
    )
    hidden_out = lax.dot_general(
        perm3, back, (((0, 1), (0, 1)), ((), ())), preferred_element_type=jnp.float32
    ).astype(jnp.bfloat16)
    return (hidden_out, kv_moved)


def solution(mesh):
    placed = (
        P("ep", "dp"),
        P("ep", None),
        P("ep", "dp"),
        P("ep"),
        P("ep", None),
        P("dp", None),
        P(),
        P(),
        P(("ep", "dp"), None, None),
        P(("ep", "dp"), None, None),
        P(("ep", "dp"), None, None),
        P(),
    )
    return jax.shard_map(
        local, mesh=mesh, in_specs=placed, out_specs=(P("ep", "dp"), P("ep", "dp")), check_vma=False
    )
```

```python
import jax
import jax.numpy as jnp
from jax import lax
from jax.sharding import PartitionSpec as P

epsilon = 1e-06


def local(
    context,
    residual,
    kv_new,
    moved_to,
    choices,
    o_weight,
    gain_mid,
    router_weight,
    w_gate,
    w_up,
    w_down,
    gain_out,
):
    peer_count = lax.axis_size("ep")
    dp_count = lax.axis_size("dp")
    my_side = lax.axis_index("dp")
    row_count = moved_to.shape[0]
    share_rows = row_count // peer_count
    model_width = gain_out.shape[0]
    col_width = model_width // dp_count
    expert_count = router_weight.shape[1]
    top_count = choices.shape[1]
    capacity = 2 * row_count * top_count // expert_count
    slot_limit = peer_count * capacity
    my_index = lax.axis_index("ep")

    def swap(x):
        return lax.ppermute(x, "dp", [(0, 1), (1, 0)])

    def own_cols(x):
        return lax.dynamic_slice_in_dim(x, my_side * col_width, col_width, 1)

    def other_cols(x):
        return lax.dynamic_slice_in_dim(x, (1 - my_side) * col_width, col_width, 1)

    partial = jnp.dot(context, o_weight, preferred_element_type=jnp.float32)
    summed = own_cols(partial) + swap(other_cols(partial))
    res_cols = lax.dynamic_slice_in_dim(residual, my_side * col_width, col_width, 1)
    stream_half = (res_cols.astype(jnp.float32) + summed).astype(jnp.bfloat16)

    target = moved_to // row_count
    placed = target * share_rows + moved_to % row_count - my_index * share_rows
    lanes = jnp.arange(row_count, dtype=jnp.int32)
    slots = lanes.reshape(peer_count, share_rows)
    perm3 = (placed[None, None, :] == slots[:, :, None]).astype(jnp.bfloat16)
    payload = jnp.concatenate([stream_half, kv_new], axis=1)
    packed = lax.dot_general(
        perm3, payload, (((2,), (0,)), ((), ())), preferred_element_type=jnp.float32
    ).astype(jnp.bfloat16)
    moved = lax.all_to_all(packed, "ep", 0, 0, tiled=True).reshape(row_count, -1)
    side_experts = jnp.arange(peer_count, dtype=jnp.int32) * dp_count + my_side
    match = choices[:, :, None] == side_experts[None, None, :]
    mine = jnp.any(match, axis=1)
    earlier = (lanes[None, :] < lanes[:, None]).astype(jnp.bfloat16)
    before = jnp.dot(earlier, mine.astype(jnp.bfloat16), preferred_element_type=jnp.float32)
    rank_iota = jnp.arange(capacity, dtype=jnp.float32)
    route3 = mine[:, :, None] & (before[:, :, None] == rank_iota[None, None, :])
    route = route3.reshape(row_count, slot_limit).astype(jnp.bfloat16)
    moved, route = lax.optimization_barrier((moved, route))
    stream_mine = moved[:, :col_width]
    kv_moved = moved[:, col_width:]
    stream_other = swap(stream_mine)
    stream = jnp.where(
        my_side == 0,
        jnp.concatenate([stream_mine, stream_other], axis=1),
        jnp.concatenate([stream_other, stream_mine], axis=1),
    )

    stream_f = stream.astype(jnp.float32)
    normed = (
        stream_f
        * lax.rsqrt(jnp.mean(stream_f * stream_f, axis=-1, keepdims=True) + epsilon)
        * gain_mid
    ).astype(jnp.bfloat16)
    logits = jnp.dot(normed, router_weight, preferred_element_type=jnp.float32)
    expert_iota = jnp.arange(expert_count, dtype=jnp.int32)
    onehot_bool = choices[:, :, None] == expert_iota[None, None, :]
    picked = jnp.sum(jnp.where(onehot_bool, logits[:, None, :], 0.0), axis=2)
    scores = jnp.exp(picked)
    mixing = scores / jnp.sum(scores, axis=1, keepdims=True)

    outgoing = lax.dot_general(
        route, normed, (((0,), (0,)), ((), ())), preferred_element_type=jnp.float32
    ).astype(jnp.bfloat16)

    arrived = lax.all_to_all(
        outgoing.reshape(peer_count, capacity, model_width), "ep", 0, 0, tiled=True
    )
    flat_rows = arrived.reshape(-1, model_width)
    gate_out = jnp.dot(flat_rows, w_gate[0], preferred_element_type=jnp.float32)
    up_out = jnp.dot(flat_rows, w_up[0], preferred_element_type=jnp.float32)
    active = lax.optimization_barrier((jax.nn.silu(gate_out) * up_out).astype(jnp.bfloat16))
    expert_out = jnp.dot(active, w_down[0], preferred_element_type=jnp.float32).astype(jnp.bfloat16)
    returned = lax.all_to_all(
        expert_out.reshape(arrived.shape), "ep", 0, 0, tiled=True
    ).reshape(slot_limit, model_width)

    chosen_mix = jnp.sum(jnp.where(match, mixing[:, :, None], 0.0), axis=1)
    weights = jnp.where(route3, chosen_mix[:, :, None], 0.0).reshape(row_count, slot_limit)
    moe_part = jnp.dot(
        weights.astype(jnp.bfloat16), returned, preferred_element_type=jnp.float32
    )
    moe_other = swap(moe_part.astype(jnp.bfloat16))
    combined_full = stream_f + moe_part + moe_other.astype(jnp.float32)
    square_sum = jnp.sum(combined_full * combined_full, axis=-1, keepdims=True)
    combined = own_cols(combined_full)
    gain_cols = lax.dynamic_slice_in_dim(gain_out, my_side * col_width, col_width, 0)
    result_cols = (
        combined * lax.rsqrt(square_sum / model_width + epsilon) * gain_cols
    ).astype(jnp.bfloat16)
    back = lax.all_to_all(
        result_cols.reshape(peer_count, share_rows, col_width), "ep", 0, 0, tiled=True
    )
    hidden_out = lax.dot_general(
        perm3, back, (((0, 1), (0, 1)), ((), ())), preferred_element_type=jnp.float32
    ).astype(jnp.bfloat16)
    return (hidden_out, kv_moved)


def solution(mesh):
    placed = (
        P("ep", "dp"),
        P("ep", None),
        P("ep", "dp"),
        P("ep"),
        P("ep", None),
        P("dp", None),
        P(),
        P(),
        P(("ep", "dp"), None, None),
        P(("ep", "dp"), None, None),
        P(("ep", "dp"), None, None),
        P(),
    )
    return jax.shard_map(
        local, mesh=mesh, in_specs=placed, out_specs=(P("ep", "dp"), P("ep", "dp")), check_vma=False
    )
```

```python
import jax
import jax.numpy as jnp
from jax import lax
from jax.sharding import PartitionSpec as P

epsilon = 1e-06


def local(
    context,
    residual,
    kv_new,
    moved_to,
    choices,
    o_weight,
    gain_mid,
    router_weight,
    w_gate,
    w_up,
    w_down,
    gain_out,
):
    peer_count = lax.axis_size("ep")
    dp_count = lax.axis_size("dp")
    my_side = lax.axis_index("dp")
    row_count = moved_to.shape[0]
    share_rows = row_count // peer_count
    model_width = gain_out.shape[0]
    col_width = model_width // dp_count
    expert_count = router_weight.shape[1]
    top_count = choices.shape[1]
    capacity = 2 * row_count * top_count // expert_count
    slot_limit = peer_count * capacity
    my_index = lax.axis_index("ep")

    def swap(x):
        return lax.ppermute(x, "dp", [(0, 1), (1, 0)])

    def own_cols(x):
        return lax.dynamic_slice_in_dim(x, my_side * col_width, col_width, 1)

    def other_cols(x):
        return lax.dynamic_slice_in_dim(x, (1 - my_side) * col_width, col_width, 1)

    partial = jnp.dot(context, o_weight, preferred_element_type=jnp.float32)
    summed = own_cols(partial) + swap(other_cols(partial))
    res_cols = lax.dynamic_slice_in_dim(residual, my_side * col_width, col_width, 1)
    stream_half = (res_cols.astype(jnp.float32) + summed).astype(jnp.bfloat16)

    target = moved_to // row_count
    placed = target * share_rows + moved_to % row_count - my_index * share_rows
    lanes = jnp.arange(row_count, dtype=jnp.int32)
    slots = lanes.reshape(peer_count, share_rows)
    perm3 = (placed[None, None, :] == slots[:, :, None]).astype(jnp.bfloat16)
    payload = jnp.concatenate([stream_half, kv_new], axis=1)
    packed = lax.dot_general(
        perm3, payload, (((2,), (0,)), ((), ())), preferred_element_type=jnp.float32
    ).astype(jnp.bfloat16)
    moved = lax.all_to_all(packed, "ep", 0, 0, tiled=True).reshape(row_count, -1)
    side_experts = jnp.arange(peer_count, dtype=jnp.int32) * dp_count + my_side
    match = choices[:, :, None] == side_experts[None, None, :]
    mine = jnp.any(match, axis=1)
    earlier = (lanes[None, :] < lanes[:, None]).astype(jnp.bfloat16)
    before = jnp.dot(earlier, mine.astype(jnp.bfloat16), preferred_element_type=jnp.float32)
    rank_iota = jnp.arange(capacity, dtype=jnp.float32)
    route3 = mine[:, :, None] & (before[:, :, None] == rank_iota[None, None, :])
    route = route3.reshape(row_count, slot_limit).astype(jnp.bfloat16)
    moved, route = lax.optimization_barrier((moved, route))
    stream_mine = moved[:, :col_width]
    kv_moved = moved[:, col_width:]
    stream_other = swap(stream_mine)
    stream = jnp.where(
        my_side == 0,
        jnp.concatenate([stream_mine, stream_other], axis=1),
        jnp.concatenate([stream_other, stream_mine], axis=1),
    )

    stream_f = stream.astype(jnp.float32)
    normed = (
        stream_f
        * lax.rsqrt(jnp.mean(stream_f * stream_f, axis=-1, keepdims=True) + epsilon)
        * gain_mid
    ).astype(jnp.bfloat16)
    normed = lax.optimization_barrier(normed)
    logits = jnp.dot(normed, router_weight, preferred_element_type=jnp.float32)
    expert_iota = jnp.arange(expert_count, dtype=jnp.int32)
    onehot_bool = choices[:, :, None] == expert_iota[None, None, :]
    picked = jnp.sum(jnp.where(onehot_bool, logits[:, None, :], 0.0), axis=2)
    scores = jnp.exp(picked)
    mixing = scores / jnp.sum(scores, axis=1, keepdims=True)

    outgoing = lax.dot_general(
        route, normed, (((0,), (0,)), ((), ())), preferred_element_type=jnp.float32
    ).astype(jnp.bfloat16)

    arrived = lax.all_to_all(
        outgoing.reshape(peer_count, capacity, model_width), "ep", 0, 0, tiled=True
    )
    flat_rows = arrived.reshape(-1, model_width)
    gate_out = jnp.dot(flat_rows, w_gate[0], preferred_element_type=jnp.float32)
    up_out = jnp.dot(flat_rows, w_up[0], preferred_element_type=jnp.float32)
    active = lax.optimization_barrier((jax.nn.silu(gate_out) * up_out).astype(jnp.bfloat16))
    expert_out = jnp.dot(active, w_down[0], preferred_element_type=jnp.float32).astype(jnp.bfloat16)
    returned = lax.all_to_all(
        expert_out.reshape(arrived.shape), "ep", 0, 0, tiled=True
    ).reshape(slot_limit, model_width)

    chosen_mix = jnp.sum(jnp.where(match, mixing[:, :, None], 0.0), axis=1)
    weights = jnp.where(route3, chosen_mix[:, :, None], 0.0).reshape(row_count, slot_limit)
    weights = lax.optimization_barrier(weights.astype(jnp.bfloat16))
    moe_part = jnp.dot(weights, returned, preferred_element_type=jnp.float32)
    moe_other = swap(moe_part.astype(jnp.bfloat16))
    combined_full = stream_f + moe_part + moe_other.astype(jnp.float32)
    square_sum = jnp.sum(combined_full * combined_full, axis=-1, keepdims=True)
    combined = own_cols(combined_full)
    gain_cols = lax.dynamic_slice_in_dim(gain_out, my_side * col_width, col_width, 0)
    result_cols = (
        combined * lax.rsqrt(square_sum / model_width + epsilon) * gain_cols
    ).astype(jnp.bfloat16)
    back = lax.all_to_all(
        result_cols.reshape(peer_count, share_rows, col_width), "ep", 0, 0, tiled=True
    )
    hidden_out = lax.dot_general(
        perm3, back, (((0, 1), (0, 1)), ((), ())), preferred_element_type=jnp.float32
    ).astype(jnp.bfloat16)
    return (hidden_out, kv_moved)


def solution(mesh):
    placed = (
        P("ep", "dp"),
        P("ep", None),
        P("ep", "dp"),
        P("ep"),
        P("ep", None),
        P("dp", None),
        P(),
        P(),
        P(("ep", "dp"), None, None),
        P(("ep", "dp"), None, None),
        P(("ep", "dp"), None, None),
        P(),
    )
    return jax.shard_map(
        local, mesh=mesh, in_specs=placed, out_specs=(P("ep", "dp"), P("ep", "dp")), check_vma=False
    )
```

```python
import jax
import jax.numpy as jnp
from jax import lax
from jax.sharding import PartitionSpec as P

epsilon = 1e-06


def local(
    context,
    residual,
    kv_new,
    moved_to,
    choices,
    o_weight,
    gain_mid,
    router_weight,
    w_gate,
    w_up,
    w_down,
    gain_out,
):
    peer_count = lax.axis_size("ep")
    dp_count = lax.axis_size("dp")
    my_side = lax.axis_index("dp")
    row_count = moved_to.shape[0]
    share_rows = row_count // peer_count
    model_width = gain_out.shape[0]
    col_width = model_width // dp_count
    expert_count = router_weight.shape[1]
    top_count = choices.shape[1]
    capacity = 2 * row_count * top_count // expert_count
    slot_limit = peer_count * capacity
    my_index = lax.axis_index("ep")

    def swap(x):
        return lax.ppermute(x, "dp", [(0, 1), (1, 0)])

    def own_cols(x):
        return lax.dynamic_slice_in_dim(x, my_side * col_width, col_width, 1)

    def other_cols(x):
        return lax.dynamic_slice_in_dim(x, (1 - my_side) * col_width, col_width, 1)

    partial_t = lax.dot_general(
        o_weight, context, (((0,), (1,)), ((), ())), preferred_element_type=jnp.float32
    )
    own_t = lax.dynamic_slice_in_dim(partial_t, my_side * col_width, col_width, 0)
    other_t = lax.dynamic_slice_in_dim(partial_t, (1 - my_side) * col_width, col_width, 0)
    summed = (own_t + swap(other_t)).T
    res_cols = lax.dynamic_slice_in_dim(residual, my_side * col_width, col_width, 1)
    stream_half = (res_cols.astype(jnp.float32) + summed).astype(jnp.bfloat16)

    target = moved_to // row_count
    placed = target * share_rows + moved_to % row_count - my_index * share_rows
    lanes = jnp.arange(row_count, dtype=jnp.int32)
    slots = lanes.reshape(peer_count, share_rows)
    perm3 = (placed[None, None, :] == slots[:, :, None]).astype(jnp.bfloat16)
    payload = jnp.concatenate([stream_half, kv_new], axis=1)
    packed = lax.dot_general(
        perm3, payload, (((2,), (0,)), ((), ())), preferred_element_type=jnp.float32
    ).astype(jnp.bfloat16)
    moved = lax.all_to_all(packed, "ep", 0, 0, tiled=True).reshape(row_count, -1)
    side_experts = jnp.arange(peer_count, dtype=jnp.int32) * dp_count + my_side
    match = choices[:, :, None] == side_experts[None, None, :]
    mine = jnp.any(match, axis=1)
    earlier = (lanes[None, :] < lanes[:, None]).astype(jnp.bfloat16)
    before = jnp.dot(earlier, mine.astype(jnp.bfloat16), preferred_element_type=jnp.float32)
    rank_iota = jnp.arange(capacity, dtype=jnp.float32)
    route3 = mine[:, :, None] & (before[:, :, None] == rank_iota[None, None, :])
    route = route3.reshape(row_count, slot_limit).astype(jnp.bfloat16)
    moved, route = lax.optimization_barrier((moved, route))
    stream_mine = moved[:, :col_width]
    kv_moved = moved[:, col_width:]
    stream_other = swap(stream_mine)
    stream = jnp.where(
        my_side == 0,
        jnp.concatenate([stream_mine, stream_other], axis=1),
        jnp.concatenate([stream_other, stream_mine], axis=1),
    )

    stream_f = stream.astype(jnp.float32)
    normed = (
        stream_f
        * lax.rsqrt(jnp.mean(stream_f * stream_f, axis=-1, keepdims=True) + epsilon)
        * gain_mid
    ).astype(jnp.bfloat16)
    logits = jnp.dot(normed, router_weight, preferred_element_type=jnp.float32)
    expert_iota = jnp.arange(expert_count, dtype=jnp.int32)
    onehot_bool = choices[:, :, None] == expert_iota[None, None, :]
    picked = jnp.sum(jnp.where(onehot_bool, logits[:, None, :], 0.0), axis=2)
    scores = jnp.exp(picked)
    mixing = scores / jnp.sum(scores, axis=1, keepdims=True)

    outgoing = lax.dot_general(
        route, normed, (((0,), (0,)), ((), ())), preferred_element_type=jnp.float32
    ).astype(jnp.bfloat16)

    arrived = lax.all_to_all(
        outgoing.reshape(peer_count, capacity, model_width), "ep", 0, 0, tiled=True
    )
    flat_rows = arrived.reshape(-1, model_width)
    gate_out = jnp.dot(flat_rows, w_gate[0], preferred_element_type=jnp.float32)
    up_out = jnp.dot(flat_rows, w_up[0], preferred_element_type=jnp.float32)
    active = lax.optimization_barrier((jax.nn.silu(gate_out) * up_out).astype(jnp.bfloat16))
    expert_out = jnp.dot(active, w_down[0], preferred_element_type=jnp.float32).astype(jnp.bfloat16)
    returned = lax.all_to_all(
        expert_out.reshape(arrived.shape), "ep", 0, 0, tiled=True
    ).reshape(slot_limit, model_width)

    chosen_mix = jnp.sum(jnp.where(match, mixing[:, :, None], 0.0), axis=1)
    weights = jnp.where(route3, chosen_mix[:, :, None], 0.0).reshape(row_count, slot_limit)
    moe_part = jnp.dot(
        weights.astype(jnp.bfloat16), returned, preferred_element_type=jnp.float32
    )
    moe_other = swap(moe_part.astype(jnp.bfloat16))
    combined_full = stream_f + moe_part + moe_other.astype(jnp.float32)
    square_sum = jnp.sum(combined_full * combined_full, axis=-1, keepdims=True)
    combined = own_cols(combined_full)
    gain_cols = lax.dynamic_slice_in_dim(gain_out, my_side * col_width, col_width, 0)
    result_cols = (
        combined * lax.rsqrt(square_sum / model_width + epsilon) * gain_cols
    ).astype(jnp.bfloat16)
    back = lax.all_to_all(
        result_cols.reshape(peer_count, share_rows, col_width), "ep", 0, 0, tiled=True
    )
    hidden_out = lax.dot_general(
        perm3, back, (((0, 1), (0, 1)), ((), ())), preferred_element_type=jnp.float32
    ).astype(jnp.bfloat16)
    return (hidden_out, kv_moved)


def solution(mesh):
    placed = (
        P("ep", "dp"),
        P("ep", None),
        P("ep", "dp"),
        P("ep"),
        P("ep", None),
        P("dp", None),
        P(),
        P(),
        P(("ep", "dp"), None, None),
        P(("ep", "dp"), None, None),
        P(("ep", "dp"), None, None),
        P(),
    )
    return jax.shard_map(
        local, mesh=mesh, in_specs=placed, out_specs=(P("ep", "dp"), P("ep", "dp")), check_vma=False
    )
```

```python
import jax
import jax.numpy as jnp
from jax import lax
from jax.sharding import PartitionSpec as P

epsilon = 1e-06


def local(
    context,
    residual,
    kv_new,
    moved_to,
    choices,
    o_weight,
    gain_mid,
    router_weight,
    w_gate,
    w_up,
    w_down,
    gain_out,
):
    peer_count = lax.axis_size("ep")
    dp_count = lax.axis_size("dp")
    my_side = lax.axis_index("dp")
    row_count = moved_to.shape[0]
    share_rows = row_count // peer_count
    model_width = gain_out.shape[0]
    col_width = model_width // dp_count
    expert_count = router_weight.shape[1]
    top_count = choices.shape[1]
    capacity = 2 * row_count * top_count // expert_count
    slot_limit = peer_count * capacity
    my_index = lax.axis_index("ep")

    def swap(x):
        return lax.ppermute(x, "dp", [(0, 1), (1, 0)])

    def own_cols(x):
        return lax.dynamic_slice_in_dim(x, my_side * col_width, col_width, 1)

    def other_cols(x):
        return lax.dynamic_slice_in_dim(x, (1 - my_side) * col_width, col_width, 1)

    partial = jnp.dot(context, o_weight, preferred_element_type=jnp.float32)
    summed = own_cols(partial) + swap(other_cols(partial))
    res_cols = lax.dynamic_slice_in_dim(residual, my_side * col_width, col_width, 1)
    stream_half = (res_cols.astype(jnp.float32) + summed).astype(jnp.bfloat16)

    target = moved_to // row_count
    placed = target * share_rows + moved_to % row_count - my_index * share_rows
    lanes = jnp.arange(row_count, dtype=jnp.int32)
    slots = lanes.reshape(peer_count, share_rows)
    perm3 = (placed[None, None, :] == slots[:, :, None]).astype(jnp.bfloat16)
    payload = jnp.concatenate([stream_half, kv_new], axis=1)
    packed = lax.dot_general(
        perm3, payload, (((2,), (0,)), ((), ())), preferred_element_type=jnp.float32
    ).astype(jnp.bfloat16)
    moved = lax.all_to_all(packed, "ep", 0, 0, tiled=True)
    side_experts = jnp.arange(peer_count, dtype=jnp.int32) * dp_count + my_side
    match = choices[:, :, None] == side_experts[None, None, :]
    mine = jnp.any(match, axis=1)
    earlier = (lanes[None, :] < lanes[:, None]).astype(jnp.bfloat16)
    before = jnp.dot(earlier, mine.astype(jnp.bfloat16), preferred_element_type=jnp.float32)
    rank_iota = jnp.arange(capacity, dtype=jnp.float32)
    route3 = mine[:, :, None] & (before[:, :, None] == rank_iota[None, None, :])
    route = route3.reshape(row_count, slot_limit).astype(jnp.bfloat16)
    moved, route = lax.optimization_barrier((moved, route))
    stream_mine = moved[:, :, :col_width].reshape(row_count, col_width)
    kv_moved = moved[:, :, col_width:].reshape(row_count, -1)
    stream_other = swap(stream_mine)
    stream = jnp.where(
        my_side == 0,
        jnp.concatenate([stream_mine, stream_other], axis=1),
        jnp.concatenate([stream_other, stream_mine], axis=1),
    )

    stream_f = stream.astype(jnp.float32)
    normed = (
        stream_f
        * lax.rsqrt(jnp.mean(stream_f * stream_f, axis=-1, keepdims=True) + epsilon)
        * gain_mid
    ).astype(jnp.bfloat16)
    logits = jnp.dot(normed, router_weight, preferred_element_type=jnp.float32)
    expert_iota = jnp.arange(expert_count, dtype=jnp.int32)
    onehot_bool = choices[:, :, None] == expert_iota[None, None, :]
    picked = jnp.sum(jnp.where(onehot_bool, logits[:, None, :], 0.0), axis=2)
    scores = jnp.exp(picked)
    mixing = scores / jnp.sum(scores, axis=1, keepdims=True)

    outgoing = lax.dot_general(
        route, normed, (((0,), (0,)), ((), ())), preferred_element_type=jnp.float32
    ).astype(jnp.bfloat16)

    arrived = lax.all_to_all(
        outgoing.reshape(peer_count, capacity, model_width), "ep", 0, 0, tiled=True
    )
    flat_rows = arrived.reshape(-1, model_width)
    gate_out = jnp.dot(flat_rows, w_gate[0], preferred_element_type=jnp.float32)
    up_out = jnp.dot(flat_rows, w_up[0], preferred_element_type=jnp.float32)
    active = lax.optimization_barrier((jax.nn.silu(gate_out) * up_out).astype(jnp.bfloat16))
    expert_out = jnp.dot(active, w_down[0], preferred_element_type=jnp.float32).astype(jnp.bfloat16)
    returned = lax.all_to_all(
        expert_out.reshape(arrived.shape), "ep", 0, 0, tiled=True
    ).reshape(slot_limit, model_width)

    chosen_mix = jnp.sum(jnp.where(match, mixing[:, :, None], 0.0), axis=1)
    weights = jnp.where(route3, chosen_mix[:, :, None], 0.0).reshape(row_count, slot_limit)
    moe_part = jnp.dot(
        weights.astype(jnp.bfloat16), returned, preferred_element_type=jnp.float32
    )
    moe_other = swap(moe_part.astype(jnp.bfloat16))
    combined_full = stream_f + moe_part + moe_other.astype(jnp.float32)
    square_sum = jnp.sum(combined_full * combined_full, axis=-1, keepdims=True)
    combined = own_cols(combined_full)
    gain_cols = lax.dynamic_slice_in_dim(gain_out, my_side * col_width, col_width, 0)
    result_cols = (
        combined * lax.rsqrt(square_sum / model_width + epsilon) * gain_cols
    ).astype(jnp.bfloat16)
    back = lax.all_to_all(
        result_cols.reshape(peer_count, share_rows, col_width), "ep", 0, 0, tiled=True
    )
    hidden_out = lax.dot_general(
        perm3, back, (((0, 1), (0, 1)), ((), ())), preferred_element_type=jnp.float32
    ).astype(jnp.bfloat16)
    return (hidden_out, kv_moved)


def solution(mesh):
    placed = (
        P("ep", "dp"),
        P("ep", None),
        P("ep", "dp"),
        P("ep"),
        P("ep", None),
        P("dp", None),
        P(),
        P(),
        P(("ep", "dp"), None, None),
        P(("ep", "dp"), None, None),
        P(("ep", "dp"), None, None),
        P(),
    )
    return jax.shard_map(
        local, mesh=mesh, in_specs=placed, out_specs=(P("ep", "dp"), P("ep", "dp")), check_vma=False
    )
```

```python
import jax
import jax.numpy as jnp
from jax import lax
from jax.sharding import PartitionSpec as P

epsilon = 1e-06


def local(
    context,
    residual,
    kv_new,
    moved_to,
    choices,
    o_weight,
    gain_mid,
    router_weight,
    w_gate,
    w_up,
    w_down,
    gain_out,
):
    peer_count = lax.axis_size("ep")
    dp_count = lax.axis_size("dp")
    my_side = lax.axis_index("dp")
    row_count = moved_to.shape[0]
    share_rows = row_count // peer_count
    model_width = gain_out.shape[0]
    col_width = model_width // dp_count
    expert_count = router_weight.shape[1]
    top_count = choices.shape[1]
    capacity = 2 * row_count * top_count // expert_count
    slot_limit = peer_count * capacity
    my_index = lax.axis_index("ep")

    def swap(x):
        return lax.ppermute(x, "dp", [(0, 1), (1, 0)])

    def own_cols(x):
        return lax.dynamic_slice_in_dim(x, my_side * col_width, col_width, 1)

    def other_cols(x):
        return lax.dynamic_slice_in_dim(x, (1 - my_side) * col_width, col_width, 1)

    partial = jnp.dot(context, o_weight, preferred_element_type=jnp.float32)
    summed = own_cols(partial) + swap(other_cols(partial).astype(jnp.bfloat16)).astype(jnp.float32)
    res_cols = lax.dynamic_slice_in_dim(residual, my_side * col_width, col_width, 1)
    stream_half = (res_cols.astype(jnp.float32) + summed).astype(jnp.bfloat16)

    target = moved_to // row_count
    placed = target * share_rows + moved_to % row_count - my_index * share_rows
    lanes = jnp.arange(row_count, dtype=jnp.int32)
    slots = lanes.reshape(peer_count, share_rows)
    perm3 = (placed[None, None, :] == slots[:, :, None]).astype(jnp.bfloat16)
    payload = jnp.concatenate([stream_half, kv_new], axis=1)
    packed = lax.dot_general(
        perm3, payload, (((2,), (0,)), ((), ())), preferred_element_type=jnp.float32
    ).astype(jnp.bfloat16)
    moved = lax.all_to_all(packed, "ep", 0, 0, tiled=True).reshape(row_count, -1)
    side_experts = jnp.arange(peer_count, dtype=jnp.int32) * dp_count + my_side
    match = choices[:, :, None] == side_experts[None, None, :]
    mine = jnp.any(match, axis=1)
    earlier = (lanes[None, :] < lanes[:, None]).astype(jnp.bfloat16)
    before = jnp.dot(earlier, mine.astype(jnp.bfloat16), preferred_element_type=jnp.float32)
    rank_iota = jnp.arange(capacity, dtype=jnp.float32)
    route3 = mine[:, :, None] & (before[:, :, None] == rank_iota[None, None, :])
    route = route3.reshape(row_count, slot_limit).astype(jnp.bfloat16)
    moved, route = lax.optimization_barrier((moved, route))
    stream_mine = moved[:, :col_width]
    kv_moved = moved[:, col_width:]
    stream_other = swap(stream_mine)
    stream = jnp.where(
        my_side == 0,
        jnp.concatenate([stream_mine, stream_other], axis=1),
        jnp.concatenate([stream_other, stream_mine], axis=1),
    )

    stream_f = stream.astype(jnp.float32)
    normed = (
        stream_f
        * lax.rsqrt(jnp.mean(stream_f * stream_f, axis=-1, keepdims=True) + epsilon)
        * gain_mid
    ).astype(jnp.bfloat16)
    logits = jnp.dot(normed, router_weight, preferred_element_type=jnp.float32)
    expert_iota = jnp.arange(expert_count, dtype=jnp.int32)
    onehot_bool = choices[:, :, None] == expert_iota[None, None, :]
    picked = jnp.sum(jnp.where(onehot_bool, logits[:, None, :], 0.0), axis=2)
    scores = jnp.exp(picked)
    mixing = scores / jnp.sum(scores, axis=1, keepdims=True)

    outgoing = lax.dot_general(
        route, normed, (((0,), (0,)), ((), ())), preferred_element_type=jnp.float32
    ).astype(jnp.bfloat16)

    arrived = lax.all_to_all(
        outgoing.reshape(peer_count, capacity, model_width), "ep", 0, 0, tiled=True
    )
    flat_rows = arrived.reshape(-1, model_width)
    gate_out = jnp.dot(flat_rows, w_gate[0], preferred_element_type=jnp.float32)
    up_out = jnp.dot(flat_rows, w_up[0], preferred_element_type=jnp.float32)
    active = lax.optimization_barrier((jax.nn.silu(gate_out) * up_out).astype(jnp.bfloat16))
    expert_out = jnp.dot(active, w_down[0], preferred_element_type=jnp.float32).astype(jnp.bfloat16)
    returned = lax.all_to_all(
        expert_out.reshape(arrived.shape), "ep", 0, 0, tiled=True
    ).reshape(slot_limit, model_width)

    chosen_mix = jnp.sum(jnp.where(match, mixing[:, :, None], 0.0), axis=1)
    weights = jnp.where(route3, chosen_mix[:, :, None], 0.0).reshape(row_count, slot_limit)
    moe_part = jnp.dot(
        weights.astype(jnp.bfloat16), returned, preferred_element_type=jnp.float32
    )
    moe_other = swap(moe_part.astype(jnp.bfloat16))
    combined_full = stream_f + moe_part + moe_other.astype(jnp.float32)
    square_sum = jnp.sum(combined_full * combined_full, axis=-1, keepdims=True)
    combined = own_cols(combined_full)
    gain_cols = lax.dynamic_slice_in_dim(gain_out, my_side * col_width, col_width, 0)
    result_cols = (
        combined * lax.rsqrt(square_sum / model_width + epsilon) * gain_cols
    ).astype(jnp.bfloat16)
    back = lax.all_to_all(
        result_cols.reshape(peer_count, share_rows, col_width), "ep", 0, 0, tiled=True
    )
    hidden_out = lax.dot_general(
        perm3, back, (((0, 1), (0, 1)), ((), ())), preferred_element_type=jnp.float32
    ).astype(jnp.bfloat16)
    return (hidden_out, kv_moved)


def solution(mesh):
    placed = (
        P("ep", "dp"),
        P("ep", None),
        P("ep", "dp"),
        P("ep"),
        P("ep", None),
        P("dp", None),
        P(),
        P(),
        P(("ep", "dp"), None, None),
        P(("ep", "dp"), None, None),
        P(("ep", "dp"), None, None),
        P(),
    )
    return jax.shard_map(
        local, mesh=mesh, in_specs=placed, out_specs=(P("ep", "dp"), P("ep", "dp")), check_vma=False
    )
```

```python
import jax
import jax.numpy as jnp
from jax import lax
from jax.sharding import PartitionSpec as P

epsilon = 1e-06


def local(
    context,
    residual,
    kv_new,
    moved_to,
    choices,
    o_weight,
    gain_mid,
    router_weight,
    w_gate,
    w_up,
    w_down,
    gain_out,
):
    peer_count = lax.axis_size("ep")
    dp_count = lax.axis_size("dp")
    my_side = lax.axis_index("dp")
    row_count = moved_to.shape[0]
    share_rows = row_count // peer_count
    model_width = gain_out.shape[0]
    col_width = model_width // dp_count
    expert_count = router_weight.shape[1]
    top_count = choices.shape[1]
    capacity = 2 * row_count * top_count // expert_count
    slot_limit = peer_count * capacity
    my_index = lax.axis_index("ep")

    def swap(x):
        return lax.ppermute(x, "dp", [(0, 1), (1, 0)])

    def own_cols(x):
        return lax.dynamic_slice_in_dim(x, my_side * col_width, col_width, 1)

    def other_cols(x):
        return lax.dynamic_slice_in_dim(x, (1 - my_side) * col_width, col_width, 1)

    partial = jnp.dot(context, o_weight, preferred_element_type=jnp.float32)
    summed = own_cols(partial) + swap(other_cols(partial))
    res_cols = lax.dynamic_slice_in_dim(residual, my_side * col_width, col_width, 1)
    stream_half = (res_cols.astype(jnp.float32) + summed).astype(jnp.bfloat16)

    target = moved_to // row_count
    placed = target * share_rows + moved_to % row_count - my_index * share_rows
    lanes = jnp.arange(row_count, dtype=jnp.int32)
    slots = lanes.reshape(peer_count, share_rows)
    perm3 = (placed[None, None, :] == slots[:, :, None]).astype(jnp.bfloat16)
    payload = jnp.concatenate([stream_half, kv_new], axis=1)
    packed = lax.dot_general(
        perm3, payload, (((2,), (0,)), ((), ())), preferred_element_type=jnp.float32
    ).astype(jnp.bfloat16)
    moved = lax.all_to_all(packed, "ep", 0, 0, tiled=True).reshape(row_count, -1)
    side_experts = jnp.arange(peer_count, dtype=jnp.int32) * dp_count + my_side
    match = choices[:, :, None] == side_experts[None, None, :]
    mine = jnp.any(match, axis=1)
    earlier = (lanes[None, :] < lanes[:, None]).astype(jnp.bfloat16)
    before = jnp.dot(earlier, mine.astype(jnp.bfloat16), preferred_element_type=jnp.float32)
    rank_iota = jnp.arange(capacity, dtype=jnp.float32)
    route3 = mine[:, :, None] & (before[:, :, None] == rank_iota[None, None, :])
    route = route3.reshape(row_count, slot_limit).astype(jnp.bfloat16)
    moved, route = lax.optimization_barrier((moved, route))
    stream_mine = moved[:, :col_width]
    kv_moved = moved[:, col_width:]
    stream_other = swap(stream_mine)
    stream = jnp.where(
        my_side == 0,
        jnp.concatenate([stream_mine, stream_other], axis=1),
        jnp.concatenate([stream_other, stream_mine], axis=1),
    )

    stream_f = stream.astype(jnp.float32)
    mine_f = stream_mine.astype(jnp.float32)
    other_f = stream_other.astype(jnp.float32)
    row_square = jnp.sum(mine_f * mine_f, axis=-1, keepdims=True) + jnp.sum(
        other_f * other_f, axis=-1, keepdims=True
    )
    normed = (stream_f * lax.rsqrt(row_square / model_width + epsilon) * gain_mid).astype(
        jnp.bfloat16
    )
    logits = jnp.dot(normed, router_weight, preferred_element_type=jnp.float32)
    expert_iota = jnp.arange(expert_count, dtype=jnp.int32)
    onehot_bool = choices[:, :, None] == expert_iota[None, None, :]
    picked = jnp.sum(jnp.where(onehot_bool, logits[:, None, :], 0.0), axis=2)
    scores = jnp.exp(picked)
    mixing = scores / jnp.sum(scores, axis=1, keepdims=True)

    outgoing = lax.dot_general(
        route, normed, (((0,), (0,)), ((), ())), preferred_element_type=jnp.float32
    ).astype(jnp.bfloat16)

    arrived = lax.all_to_all(
        outgoing.reshape(peer_count, capacity, model_width), "ep", 0, 0, tiled=True
    )
    flat_rows = arrived.reshape(-1, model_width)
    gate_out = jnp.dot(flat_rows, w_gate[0], preferred_element_type=jnp.float32)
    up_out = jnp.dot(flat_rows, w_up[0], preferred_element_type=jnp.float32)
    active = lax.optimization_barrier((jax.nn.silu(gate_out) * up_out).astype(jnp.bfloat16))
    expert_out = jnp.dot(active, w_down[0], preferred_element_type=jnp.float32).astype(jnp.bfloat16)
    returned = lax.all_to_all(
        expert_out.reshape(arrived.shape), "ep", 0, 0, tiled=True
    ).reshape(slot_limit, model_width)

    chosen_mix = jnp.sum(jnp.where(match, mixing[:, :, None], 0.0), axis=1)
    weights = jnp.where(route3, chosen_mix[:, :, None], 0.0).reshape(row_count, slot_limit)
    moe_part = jnp.dot(
        weights.astype(jnp.bfloat16), returned, preferred_element_type=jnp.float32
    )
    moe_other = swap(moe_part.astype(jnp.bfloat16))
    combined_full = stream_f + moe_part + moe_other.astype(jnp.float32)
    square_sum = jnp.sum(combined_full * combined_full, axis=-1, keepdims=True)
    combined = own_cols(combined_full)
    gain_cols = lax.dynamic_slice_in_dim(gain_out, my_side * col_width, col_width, 0)
    result_cols = (
        combined * lax.rsqrt(square_sum / model_width + epsilon) * gain_cols
    ).astype(jnp.bfloat16)
    back = lax.all_to_all(
        result_cols.reshape(peer_count, share_rows, col_width), "ep", 0, 0, tiled=True
    )
    hidden_out = lax.dot_general(
        perm3, back, (((0, 1), (0, 1)), ((), ())), preferred_element_type=jnp.float32
    ).astype(jnp.bfloat16)
    return (hidden_out, kv_moved)


def solution(mesh):
    placed = (
        P("ep", "dp"),
        P("ep", None),
        P("ep", "dp"),
        P("ep"),
        P("ep", None),
        P("dp", None),
        P(),
        P(),
        P(("ep", "dp"), None, None),
        P(("ep", "dp"), None, None),
        P(("ep", "dp"), None, None),
        P(),
    )
    return jax.shard_map(
        local, mesh=mesh, in_specs=placed, out_specs=(P("ep", "dp"), P("ep", "dp")), check_vma=False
    )
```
